768 devices in a mesh: ctx: 96 (over x, z, y_hi), grp: 8 (over y_lo, core).
Axes of the slice: x: 4, y: 8 (y_hi: 2, y_lo: 4; y = y_hi * 4 + y_lo), z: 12, core: 2. Of those that a mesh axis runs over, the one named last changes fastest.
Arguments:
- queries: bfloat16 [122880, 4096], P(('ctx', 'grp')), may hold values from -27 to 27
- keys: bfloat16 [122880, 512], P(('ctx', 'grp')), may hold values from -4.5 to 4.5
- values: bfloat16 [122880, 512], P(('ctx', 'grp')), may hold values from -6 to 6
- lengths: int32 [384], replicated, may hold values from 1 to 640, 122880 in all
- ssmax_scale: float32 [32], replicated, may hold values from 0.3 to 0.9
Outputs:
- attended: bfloat16 [122880, 4096], P(('ctx', 'grp'))
The draws below stay inside these ranges and needn't reach their ends.
Inputs may be any that keep to these rules, and one draw needn't show every extreme that they name: Every document has 1 to 640 tokens and one has exactly 640; the lengths sum to 122880.
All inputs are finite; a program needn't handle non-finite values.
Results may differ from the reference program's by a relative error of at most 0.0047.
Values may be sent and summed in bfloat16 or wider, within the bound.
No kernel may reach another device: no remote copies, remote signals or barrier semaphores. Data moves between devices by JAX's collectives and lax.ppermute only.
A program may use at most 32 MiB of HBM per device.

```python
import math
import jax
import jax.numpy as jnp
import numpy as np
from jax import lax

HQ = 32
HK = 4
HD = 128
TOK_DEV = 160
WIN_DEV = 4
MOST = 640
TOKENS = 122880
NDOC = 384


def joint_rows(key):
    return jnp.clip(jax.random.normal(jax.random.fold_in(key, 101), (TOKENS, HK, HD), jnp.float32), -4.0, 4.0)


def draw_keys(key, part):
    base = joint_rows(key)
    return base.reshape(TOKENS, HK * HD).astype(jnp.bfloat16)


def draw_queries(key, part):
    drawn = jnp.clip(jax.random.normal(jax.random.fold_in(key, 303), (TOKENS, HQ, HD), jnp.float32), -4.0, 4.0)
    return drawn.reshape(TOKENS, HQ * HD).astype(jnp.bfloat16)


def steps_of(stream_key, dims, cuts, low, largest):
    loudness = 1.0
    for axis_at, shards_of in cuts:
        draws = jax.random.uniform(jax.random.fold_in(jax.random.fold_in(stream_key, 6), axis_at), (shards_of,), jnp.float32, low / len(cuts), largest / len(cuts))
        loudness = loudness * jnp.repeat(jnp.exp(draws), dims[axis_at] // shards_of).reshape((-1,) + (1,) * (len(dims) - 1 - axis_at))
    return loudness


def split_up(count, total, limit, skew):
    portions = [(1 << 20) // math.isqrt(rank ** skew) + 1 for rank in range(2, count + 1)]
    spare, given = total - limit - (count - 1), [1] * (count - 1)
    while spare > 0:
        candidates = [i for i in range(count - 1) if given[i] < limit]
        whole, left = sum([portions[i] for i in candidates]), spare
        for i in candidates:
            extra = min(limit - given[i], max(1, left * portions[i] // whole), spare)
            given[i] = given[i] + extra
            spare = spare - extra
    return np.array([limit] + given)


def ragged(rng, number_of, total, bound, slope):
    if number_of == 2:
        one = jax.random.randint(rng, (), max(1, total - bound), min(bound, total - 1) + 1)
        return jnp.stack([one, total - one])
    tallies = jnp.asarray(split_up(number_of, total, bound, slope), jnp.int32)
    couples = (number_of - 1) // 2
    source_of, sink = tallies[1:1 + 2 * couples:2], tallies[2:2 + 2 * couples:2]
    margin = jnp.minimum(source_of - 1, bound - sink)
    passed = jax.random.randint(jax.random.fold_in(rng, 1), (couples,), 0, 1 << 20) % (margin + 1)
    tallies = tallies.at[1:1 + 2 * couples:2].set(source_of - passed).at[2:2 + 2 * couples:2].set(sink + passed)
    return tallies[jax.random.permutation(jax.random.fold_in(rng, 2), number_of)]


def bell_draw(rng, dims, spread, reach, cuts=(), held_as=jnp.bfloat16):
    gain = steps_of(rng, dims, cuts, -0.22, 0.18) if cuts else 1.0
    values = jax.random.normal(rng, dims, jnp.float32) * spread * gain
    return jnp.minimum(jnp.maximum(values, -reach), reach).astype(held_as)


def setup_inputs(seed: int = 0) -> dict:
    arg_keys = jax.random.split(jax.random.key(seed), 6)
    queries = draw_queries(jax.random.fold_in(arg_keys[5], 71), 0)
    keys = draw_keys(jax.random.fold_in(arg_keys[5], 71), 0)
    values = bell_draw(arg_keys[2], (TOKENS, HK * HD), 1.0, 6.0, ((0, 768),))
    lengths = ragged(arg_keys[3], NDOC, TOKENS, MOST, 2).astype(jnp.int32)
    ssmax_scale = jnp.clip(jnp.exp(jax.random.uniform(arg_keys[4], (HQ,), jnp.float32, math.log(0.3), math.log(0.9))), 0.3, 0.9)
    return {"queries": queries, "keys": keys, "values": values, "lengths": lengths, "ssmax_scale": ssmax_scale}


def attend_rows(q_rows, k_window, v_window, q_pos, k_pos, lengths, ssmax_scale):
    rows = q_rows.shape[0]
    win_width = k_window.shape[0]
    per_group = HQ // HK
    totals = jnp.cumsum(lengths, dtype=jnp.int32)
    before = totals[None, :] <= q_pos[:, None]
    doc_start = lax.optimization_barrier(jnp.sum(jnp.where(before, lengths[None, :], 0), axis=1, dtype=jnp.int32))
    visible = (q_pos - doc_start + 1).astype(jnp.float32)
    score_coef = ssmax_scale[None, :] * jnp.log(visible)[:, None] / jnp.sqrt(jnp.float32(HD))
    coef_heads = score_coef.reshape(rows, HK, per_group).transpose(1, 2, 0)[..., None]
    q_heads = q_rows.astype(jnp.float32).reshape(rows, HK, per_group, HD)
    k_heads = k_window.astype(jnp.float32).reshape(win_width, HK, HD)
    v_heads = v_window.astype(jnp.float32).reshape(win_width, HK, HD)
    scores = jnp.einsum('ikgd,jkd->kgij', q_heads, k_heads) * coef_heads
    live_mask = (k_pos[None, :] >= doc_start[:, None]) & (k_pos[None, :] <= q_pos[:, None])
    scores = jnp.where(live_mask[None, None], scores, -jnp.inf)
    top_score = lax.optimization_barrier(jnp.max(scores, axis=-1, keepdims=True))
    probs = jnp.exp(scores - top_score)
    weights = (probs / lax.optimization_barrier(jnp.sum(probs, axis=-1, keepdims=True))).astype(jnp.bfloat16)
    weights = lax.optimization_barrier(weights).astype(jnp.float32)
    mixed = jnp.einsum('kgij,jkd->ikgd', weights, v_heads)
    return mixed.reshape(rows, HQ * HD).astype(jnp.bfloat16)

def reference(queries, keys, values, lengths, ssmax_scale):
    doc_most = WIN_DEV * TOK_DEV
    blocks = TOKENS // TOK_DEV
    pad_keys = jnp.concatenate([jnp.zeros((doc_most, HK * HD), keys.dtype), keys], axis=0)
    pad_values = jnp.concatenate([jnp.zeros((doc_most, HK * HD), values.dtype), values], axis=0)

    def one_block(block_id):
        row_start = (block_id * TOK_DEV).astype(jnp.int32)
        q_rows = lax.dynamic_slice_in_dim(queries, row_start, TOK_DEV, 0)
        k_window = lax.dynamic_slice_in_dim(pad_keys, row_start, doc_most + TOK_DEV, 0)
        v_window = lax.dynamic_slice_in_dim(pad_values, row_start, doc_most + TOK_DEV, 0)
        q_pos = row_start + jnp.arange(TOK_DEV, dtype=jnp.int32)
        k_pos = row_start - doc_most + jnp.arange(doc_most + TOK_DEV, dtype=jnp.int32)
        return attend_rows(q_rows, k_window, v_window, q_pos, k_pos, lengths, ssmax_scale)
    outputs = lax.map(one_block, jnp.arange(blocks, dtype=jnp.int32))
    return outputs.reshape(TOKENS, HQ * HD)
```

```python
import jax
import jax.numpy as jnp
from jax import lax
from jax.sharding import PartitionSpec as P

HQ = 32
HK = 4
HD = 128
WIN_DEV = 4
AXES = ("ctx", "grp")


def send(x, pairs):
    return lax.ppermute(x, AXES, pairs)


def window_blocks(own):
    count = lax.axis_size("ctx") * lax.axis_size("grp")
    ahead2 = [(i, i + 2) for i in range(count - 2)]
    to_odd = [(i, i + 1) for i in range(0, count - 1, 2)]
    to_even = [(i, i - 1) for i in range(1, count, 2)]
    swap = to_odd + to_even
    back2 = send(own, ahead2)
    from_even_own = send(own, to_odd)
    back4 = send(back2, ahead2)
    swapped2 = send(back2, swap)
    from_odd4 = send(back4, to_even)
    even = lax.axis_index("grp") % 2 == 0
    back1 = jnp.where(even, swapped2, from_even_own)
    back3 = jnp.where(even, from_odd4, swapped2)
    return [back4, back3, back2, back1, own]


def body(queries, keys, values, lengths, ssmax_scale):
    tok_rows = queries.shape[0]
    slab_rows = tok_rows * lax.axis_size("grp")
    doc_most = WIN_DEV * tok_rows
    win_width = doc_most + tok_rows
    per_group = HQ // HK
    grp_index = lax.axis_index("grp")
    ctx_index = lax.axis_index("ctx")
    q_start = ctx_index * slab_rows + grp_index * tok_rows
    q_pos = q_start + jnp.arange(tok_rows, dtype=jnp.int32)
    own = jnp.concatenate([keys, values], axis=1)
    window = jnp.concatenate(window_blocks(own), axis=0)
    k_window = window[:, : HK * HD]
    v_window = window[:, HK * HD :]
    k_pos = q_start - doc_most + jnp.arange(win_width, dtype=jnp.int32)
    totals = jnp.cumsum(lengths, dtype=jnp.int32)
    before = totals[None, :] <= q_pos[:, None]
    doc_start = jnp.sum(jnp.where(before, lengths[None, :], 0), axis=1, dtype=jnp.int32)
    visible = (q_pos - doc_start + 1).astype(jnp.float32)
    score_coef = ssmax_scale[None, :] * jnp.log(visible)[:, None] / jnp.sqrt(jnp.float32(HD))
    live_mask = (k_pos[None, :] >= doc_start[:, None]) & (k_pos[None, :] <= q_pos[:, None])
    pieces = []
    for kv_head in range(HK):
        q_heads = queries[:, kv_head * per_group * HD : (kv_head + 1) * per_group * HD].reshape(
            tok_rows, per_group, HD
        )
        k_head = k_window[:, kv_head * HD : (kv_head + 1) * HD]
        v_head = v_window[:, kv_head * HD : (kv_head + 1) * HD]
        head_coef = score_coef[:, kv_head * per_group : (kv_head + 1) * per_group].T[:, :, None]
        scores = (
            jnp.einsum("igd,jd->gij", q_heads, k_head, preferred_element_type=jnp.float32)
            * head_coef
        )
        scores = jnp.where(live_mask[None], scores, -jnp.inf)
        top_score = jnp.max(scores, axis=-1, keepdims=True)
        probs = jnp.exp(scores - top_score)
        weights = (probs / jnp.sum(probs, axis=-1, keepdims=True)).astype(jnp.bfloat16)
        mixed = jnp.einsum("gij,jd->igd", weights, v_head, preferred_element_type=jnp.float32)
        pieces.append(mixed.reshape(tok_rows, per_group * HD))
    return jnp.concatenate(pieces, axis=1).astype(jnp.bfloat16)


def solution(mesh):
    return jax.shard_map(
        body,
        mesh=mesh,
        in_specs=(
            P(AXES, None),
            P(AXES, None),
            P(AXES, None),
            P(),
            P(),
        ),
        out_specs=P(AXES, None),
        check_vma=False,
    )
```

```python
import jax
import jax.numpy as jnp
from jax import lax
from jax.experimental import pallas as pl
from jax.experimental.pallas import tpu as pltpu
from jax.sharding import PartitionSpec as P

HQ = 32
HK = 4
HD = 128
WIN_DEV = 4
AXES = ("ctx", "grp")


def send(x, pairs):
    return lax.ppermute(x, AXES, pairs)


def window_blocks(own):
    count = lax.axis_size("ctx") * lax.axis_size("grp")
    ahead2 = [(i, i + 2) for i in range(count - 2)]
    to_odd = [(i, i + 1) for i in range(0, count - 1, 2)]
    to_even = [(i, i - 1) for i in range(1, count, 2)]
    swap = to_odd + to_even
    back2 = send(own, ahead2)
    from_even_own = send(own, to_odd)
    back4 = send(back2, ahead2)
    swapped2 = send(back2, swap)
    from_odd4 = send(back4, to_even)
    even = lax.axis_index("grp") % 2 == 0
    back1 = jnp.where(even, swapped2, from_even_own)
    back3 = jnp.where(even, from_odd4, swapped2)
    return [back4, back3, back2, back1, own]


def attend_kernel(coef_ref, lo_ref, q_ref, k_ref, v_ref, o_ref):
    rows, width = q_ref.shape[0], k_ref.shape[0]
    doc_most = width - rows
    col = lax.broadcasted_iota(jnp.int32, (rows, width), 1)
    row = lax.broadcasted_iota(jnp.int32, (rows, width), 0)
    live = (col >= lo_ref[...]) & (col <= row + doc_most)
    k = k_ref[...]
    v = v_ref[...]
    for g in range(HQ // HK):
        q = q_ref[:, g * HD : (g + 1) * HD]
        s = lax.dot_general(q, k, (((1,), (1,)), ((), ())), preferred_element_type=jnp.float32)
        s = jnp.where(live, s * coef_ref[g], -jnp.inf)
        m = jnp.max(s, axis=1, keepdims=True)
        p = jnp.exp(s - m)
        l = jnp.sum(p, axis=1, keepdims=True)
        w = (p / l).astype(jnp.bfloat16)
        o = jnp.dot(w, v, preferred_element_type=jnp.float32)
        o_ref[:, g * HD : (g + 1) * HD] = o.astype(o_ref.dtype)


def attend(queries, window, coef, lo, interpret=False):
    rows = queries.shape[0]
    width = window.shape[0]
    per_group = HQ // HK
    flops = 4 * HQ * rows * width * HD
    return pl.pallas_call(
        attend_kernel,
        grid=(HK,),
        in_specs=[
            pl.BlockSpec((per_group, rows, 1), lambda h: (h, 0, 0)),
            pl.BlockSpec((rows, 1), lambda h: (0, 0)),
            pl.BlockSpec((rows, per_group * HD), lambda h: (0, h)),
            pl.BlockSpec((width, HD), lambda h: (0, h)),
            pl.BlockSpec((width, HD), lambda h: (0, h + HK)),
        ],
        out_specs=pl.BlockSpec((rows, per_group * HD), lambda h: (0, h)),
        out_shape=jax.ShapeDtypeStruct((rows, HQ * HD), jnp.bfloat16),
        cost_estimate=pl.CostEstimate(
            flops=flops,
            transcendentals=HQ * rows * width,
            bytes_accessed=2 * (2 * rows * HQ * HD + width * 2 * HK * HD),
        ),
        interpret=interpret,
    )(coef, lo, queries, window, window)


def body(queries, keys, values, lengths, ssmax_scale):
    tok_rows = queries.shape[0]
    slab_rows = tok_rows * lax.axis_size("grp")
    doc_most = WIN_DEV * tok_rows
    grp_index = lax.axis_index("grp")
    ctx_index = lax.axis_index("ctx")
    q_start = ctx_index * slab_rows + grp_index * tok_rows
    q_pos = q_start + jnp.arange(tok_rows, dtype=jnp.int32)
    own = jnp.concatenate([keys, values], axis=1)
    window = jnp.concatenate(window_blocks(own), axis=0)
    totals = jnp.cumsum(lengths, dtype=jnp.int32)
    before = totals[None, :] <= q_pos[:, None]
    doc_start = jnp.sum(jnp.where(before, lengths[None, :], 0), axis=1, dtype=jnp.int32)
    visible = (q_pos - doc_start + 1).astype(jnp.float32)
    score_coef = ssmax_scale[None, :] * jnp.log(visible)[:, None] / jnp.sqrt(jnp.float32(HD))
    lo = (doc_start - (q_start - doc_most))[:, None]
    return attend(queries, window, score_coef.T[:, :, None], lo)


def solution(mesh):
    return jax.shard_map(
        body,
        mesh=mesh,
        in_specs=(
            P(AXES, None),
            P(AXES, None),
            P(AXES, None),
            P(),
            P(),
        ),
        out_specs=P(AXES, None),
        check_vma=False,
    )
```

```python
import jax
import jax.numpy as jnp
from jax import lax
from jax.experimental import pallas as pl
from jax.experimental.pallas import tpu as pltpu
from jax.sharding import PartitionSpec as P

HQ = 32
HK = 4
HD = 128
WIN_DEV = 4
AXES = ("ctx", "grp")


def send(x, pairs):
    return lax.ppermute(x, AXES, pairs)


def window_blocks(own):
    count = lax.axis_size("ctx") * lax.axis_size("grp")
    ahead2 = [(i, i + 2) for i in range(count - 2)]
    to_odd = [(i, i + 1) for i in range(0, count - 1, 2)]
    to_even = [(i, i - 1) for i in range(1, count, 2)]
    swap = to_odd + to_even
    back2 = send(own, ahead2)
    from_even_own = send(own, to_odd)
    back4 = send(back2, ahead2)
    swapped2 = send(back2, swap)
    from_odd4 = send(back4, to_even)
    even = lax.axis_index("grp") % 2 == 0
    back1 = jnp.where(even, swapped2, from_even_own)
    back3 = jnp.where(even, from_odd4, swapped2)
    return [back4, back3, back2, back1, own]


def attend_kernel(scale_ref, logv_ref, lo_ref, q_ref, *refs):
    kv_refs, o_ref = refs[:-1], refs[-1]
    blocks = len(kv_refs) // 2
    rows = q_ref.shape[0]
    width = rows * blocks
    doc_most = width - rows
    head = pl.program_id(0)
    col = lax.broadcasted_iota(jnp.int32, (rows, width), 1)
    row = lax.broadcasted_iota(jnp.int32, (rows, width), 0)
    live = (col >= lo_ref[...]) & (col <= row + doc_most)
    k = jnp.concatenate([r[...] for r in kv_refs[:blocks]], axis=0)
    v = jnp.concatenate([r[...] for r in kv_refs[blocks:]], axis=0)
    logv = logv_ref[...]
    per_group = HQ // HK
    for g in range(per_group):
        coef = scale_ref[head * per_group + g] * logv / jnp.sqrt(jnp.float32(HD))
        q = q_ref[:, g * HD : (g + 1) * HD]
        s = lax.dot_general(q, k, (((1,), (1,)), ((), ())), preferred_element_type=jnp.float32)
        s = jnp.where(live, s * coef, -jnp.inf)
        m = jnp.max(s, axis=1, keepdims=True)
        p = jnp.exp(s - m)
        l = jnp.sum(p, axis=1, keepdims=True)
        w = (p * (1.0 / l)).astype(jnp.bfloat16)
        o = jnp.dot(w, v, preferred_element_type=jnp.float32)
        o_ref[:, g * HD : (g + 1) * HD] = o.astype(o_ref.dtype)


def attend(queries, blocks, scale, logv, lo, interpret=False):
    rows = queries.shape[0]
    width = rows * len(blocks)
    per_group = HQ // HK
    flops = 4 * HQ * rows * width * HD
    small = pl.BlockSpec((rows, 1), lambda h: (0, 0))
    k_specs = [pl.BlockSpec((rows, HD), lambda h: (0, h)) for _ in blocks]
    v_specs = [pl.BlockSpec((rows, HD), lambda h: (0, h + HK)) for _ in blocks]
    return pl.pallas_call(
        attend_kernel,
        grid=(HK,),
        in_specs=[
            pl.BlockSpec(memory_space=pltpu.SMEM),
            small,
            small,
            pl.BlockSpec((rows, per_group * HD), lambda h: (0, h)),
        ]
        + k_specs
        + v_specs,
        out_specs=pl.BlockSpec((rows, per_group * HD), lambda h: (0, h)),
        out_shape=jax.ShapeDtypeStruct((rows, HQ * HD), jnp.bfloat16),
        cost_estimate=pl.CostEstimate(
            flops=flops,
            transcendentals=HQ * rows * width,
            bytes_accessed=2 * (2 * rows * HQ * HD + width * 2 * HK * HD),
        ),
        interpret=interpret,
    )(scale, logv, lo, queries, *blocks, *blocks)


def body(queries, keys, values, lengths, ssmax_scale):
    tok_rows = queries.shape[0]
    slab_rows = tok_rows * lax.axis_size("grp")
    doc_most = WIN_DEV * tok_rows
    grp_index = lax.axis_index("grp")
    ctx_index = lax.axis_index("ctx")
    q_start = ctx_index * slab_rows + grp_index * tok_rows
    q_pos = q_start + jnp.arange(tok_rows, dtype=jnp.int32)
    own = jnp.concatenate([keys, values], axis=1)
    blocks = window_blocks(own)
    totals = jnp.cumsum(lengths, dtype=jnp.int32)
    before = totals[None, :] <= q_pos[:, None]
    doc_start = jnp.sum(jnp.where(before, lengths[None, :], 0), axis=1, dtype=jnp.int32)
    visible = (q_pos - doc_start + 1).astype(jnp.float32)
    lo = (doc_start - (q_start - doc_most))[:, None]
    return attend(queries, blocks, ssmax_scale, jnp.log(visible)[:, None], lo)


def solution(mesh):
    return jax.shard_map(
        body,
        mesh=mesh,
        in_specs=(
            P(AXES, None),
            P(AXES, None),
            P(AXES, None),
            P(),
            P(),
        ),
        out_specs=P(AXES, None),
        check_vma=False,
    )
```

```python
import jax
import jax.numpy as jnp
from jax import lax
from jax.experimental import pallas as pl
from jax.experimental.pallas import tpu as pltpu
from jax.sharding import PartitionSpec as P

HQ = 32
HK = 4
HD = 128
WIN_DEV = 4
AXES = ("ctx", "grp")


def send(x, pairs):
    return lax.ppermute(x, AXES, pairs)


def window_blocks(own):
    count = lax.axis_size("ctx") * lax.axis_size("grp")
    ahead2 = [(i, i + 2) for i in range(count - 2)]
    to_odd = [(i, i + 1) for i in range(0, count - 1, 2)]
    to_even = [(i, i - 1) for i in range(1, count, 2)]
    swap = to_odd + to_even
    back2 = send(own, ahead2)
    from_even_own = send(own, to_odd)
    back4 = send(back2, ahead2)
    swapped2 = send(back2, swap)
    from_odd4 = send(back4, to_even)
    even = lax.axis_index("grp") % 2 == 0
    back1 = jnp.where(even, swapped2, from_even_own)
    back3 = jnp.where(even, from_odd4, swapped2)
    return [back4, back3, back2, back1, own]


def attend_kernel(scale_ref, logv_ref, lo_ref, q_ref, *refs):
    kv_refs, o_ref = refs[:-1], refs[-1]
    blocks = len(kv_refs) // 2
    rows = q_ref.shape[0]
    width = rows * blocks
    doc_most = width - rows
    head = pl.program_id(0)
    col = lax.broadcasted_iota(jnp.int32, (rows, width), 1)
    row = lax.broadcasted_iota(jnp.int32, (rows, width), 0)
    live = (col >= lo_ref[...]) & (col <= row + doc_most)
    k = jnp.concatenate([r[...] for r in kv_refs[:blocks]], axis=0)
    v = jnp.concatenate([r[...] for r in kv_refs[blocks:]], axis=0)
    logv = logv_ref[...]
    per_group = HQ // HK
    coef = jnp.stack(
        [scale_ref[head * per_group + g] * logv / jnp.sqrt(jnp.float32(HD)) for g in range(per_group)]
    )
    q = jnp.concatenate([q_ref[:, g * HD : (g + 1) * HD] for g in range(per_group)], axis=0)
    s = lax.dot_general(q, k, (((1,), (1,)), ((), ())), preferred_element_type=jnp.float32)
    s = jnp.where(live[None], s.reshape(per_group, rows, width) * coef, -jnp.inf)
    m = jnp.max(s, axis=2, keepdims=True)
    p = jnp.exp(s - m)
    l = jnp.sum(p, axis=2, keepdims=True)
    w = (p * (1.0 / l)).astype(jnp.bfloat16).reshape(per_group * rows, width)
    o = jnp.dot(w, v, preferred_element_type=jnp.float32)
    for g in range(per_group):
        o_ref[:, g * HD : (g + 1) * HD] = o[g * rows : (g + 1) * rows].astype(o_ref.dtype)

def attend(queries, blocks, scale, logv, lo, interpret=False):
    rows = queries.shape[0]
    width = rows * len(blocks)
    per_group = HQ // HK
    flops = 4 * HQ * rows * width * HD
    small = pl.BlockSpec((rows, 1), lambda h: (0, 0))
    k_specs = [pl.BlockSpec((rows, HD), lambda h: (0, h)) for _ in blocks]
    v_specs = [pl.BlockSpec((rows, HD), lambda h: (0, h + HK)) for _ in blocks]
    return pl.pallas_call(
        attend_kernel,
        grid=(HK,),
        in_specs=[
            pl.BlockSpec(memory_space=pltpu.SMEM),
            small,
            small,
            pl.BlockSpec((rows, per_group * HD), lambda h: (0, h)),
        ]
        + k_specs
        + v_specs,
        out_specs=pl.BlockSpec((rows, per_group * HD), lambda h: (0, h)),
        out_shape=jax.ShapeDtypeStruct((rows, HQ * HD), jnp.bfloat16),
        cost_estimate=pl.CostEstimate(
            flops=flops,
            transcendentals=HQ * rows * width,
            bytes_accessed=2 * (2 * rows * HQ * HD + width * 2 * HK * HD),
        ),
        interpret=interpret,
    )(scale, logv, lo, queries, *blocks, *blocks)


def body(queries, keys, values, lengths, ssmax_scale):
    tok_rows = queries.shape[0]
    slab_rows = tok_rows * lax.axis_size("grp")
    doc_most = WIN_DEV * tok_rows
    grp_index = lax.axis_index("grp")
    ctx_index = lax.axis_index("ctx")
    q_start = ctx_index * slab_rows + grp_index * tok_rows
    q_pos = q_start + jnp.arange(tok_rows, dtype=jnp.int32)
    own = jnp.concatenate([keys, values], axis=1)
    blocks = window_blocks(own)
    totals = jnp.cumsum(lengths, dtype=jnp.int32)
    before = totals[None, :] <= q_pos[:, None]
    doc_start = jnp.sum(jnp.where(before, lengths[None, :], 0), axis=1, dtype=jnp.int32)
    visible = (q_pos - doc_start + 1).astype(jnp.float32)
    lo = (doc_start - (q_start - doc_most))[:, None]
    return attend(queries, blocks, ssmax_scale, jnp.log(visible)[:, None], lo)


def solution(mesh):
    return jax.shard_map(
        body,
        mesh=mesh,
        in_specs=(
            P(AXES, None),
            P(AXES, None),
            P(AXES, None),
            P(),
            P(),
        ),
        out_specs=P(AXES, None),
        check_vma=False,
    )
```

```python
import jax
import jax.numpy as jnp
from jax import lax
from jax.experimental import pallas as pl
from jax.experimental.pallas import tpu as pltpu
from jax.sharding import PartitionSpec as P

HQ = 32
HK = 4
HD = 128
WIN_DEV = 4
AXES = ("ctx", "grp")


def send(x, pairs):
    return lax.ppermute(x, AXES, pairs)


def window_blocks(own):
    count = lax.axis_size("ctx") * lax.axis_size("grp")
    ahead2 = [(i, i + 2) for i in range(count - 2)]
    to_odd = [(i, i + 1) for i in range(0, count - 1, 2)]
    to_even = [(i, i - 1) for i in range(1, count, 2)]
    swap = to_odd + to_even
    back2 = send(own, ahead2)
    from_even_own = send(own, to_odd)
    back4 = send(back2, ahead2)
    swapped2 = send(back2, swap)
    from_odd4 = send(back4, to_even)
    return [back4, from_odd4, swapped2, back2, from_even_own, own]


def attend_kernel(qs_ref, scale_ref, ds_ref, q_ref, *refs):
    kv_refs, o_ref = refs[:-1], refs[-1]
    half = len(kv_refs) // 2
    rows = q_ref.shape[0]
    width = rows * (half - 1)
    doc_most = width - rows
    head = pl.program_id(0)
    q_start = qs_ref[0]
    even = qs_ref[1] == 0

    def ordered(r):
        back4, odd4, swap2, back2, even_own, own = [x[...] for x in r]
        back3 = jnp.where(even, odd4, swap2)
        back1 = jnp.where(even, swap2, even_own)
        return jnp.concatenate([back4, back3, back2, back1, own], axis=0)

    col = lax.broadcasted_iota(jnp.int32, (rows, width), 1)
    row = lax.broadcasted_iota(jnp.int32, (rows, width), 0)
    doc_start = ds_ref[...]
    live = (col >= doc_start - (q_start - doc_most)) & (col <= row + doc_most)
    k = ordered(kv_refs[:half])
    v = ordered(kv_refs[half:])
    q_pos = q_start + lax.broadcasted_iota(jnp.int32, (rows, 1), 0)
    logv = jnp.log((q_pos - doc_start + 1).astype(jnp.float32))
    per_group = HQ // HK
    coef = jnp.stack(
        [scale_ref[head * per_group + g] * logv / jnp.sqrt(jnp.float32(HD)) for g in range(per_group)]
    )
    q = jnp.concatenate([q_ref[:, g * HD : (g + 1) * HD] for g in range(per_group)], axis=0)
    s = lax.dot_general(q, k, (((1,), (1,)), ((), ())), preferred_element_type=jnp.float32)
    s = jnp.where(live[None], s.reshape(per_group, rows, width) * coef, -jnp.inf)
    m = jnp.max(s, axis=2, keepdims=True)
    p = jnp.exp(s - m)
    l = jnp.sum(p, axis=2, keepdims=True)
    w = (p * (1.0 / l)).astype(jnp.bfloat16).reshape(per_group * rows, width)
    o = jnp.dot(w, v, preferred_element_type=jnp.float32)
    for g in range(per_group):
        o_ref[:, g * HD : (g + 1) * HD] = o[g * rows : (g + 1) * rows].astype(o_ref.dtype)


def attend(queries, blocks, where, scale, doc_start, interpret=False):
    rows = queries.shape[0]
    width = rows * (len(blocks) - 1)
    per_group = HQ // HK
    flops = 4 * HQ * rows * width * HD
    k_specs = [pl.BlockSpec((rows, HD), lambda h: (0, h)) for _ in blocks]
    v_specs = [pl.BlockSpec((rows, HD), lambda h: (0, h + HK)) for _ in blocks]
    return pl.pallas_call(
        attend_kernel,
        grid=(HK,),
        in_specs=[
            pl.BlockSpec(memory_space=pltpu.SMEM),
            pl.BlockSpec(memory_space=pltpu.SMEM),
            pl.BlockSpec((rows, 1), lambda h: (0, 0)),
            pl.BlockSpec((rows, per_group * HD), lambda h: (0, h)),
        ]
        + k_specs
        + v_specs,
        out_specs=pl.BlockSpec((rows, per_group * HD), lambda h: (0, h)),
        out_shape=jax.ShapeDtypeStruct((rows, HQ * HD), jnp.bfloat16),
        cost_estimate=pl.CostEstimate(
            flops=flops,
            transcendentals=HQ * rows * width,
            bytes_accessed=2 * (2 * rows * HQ * HD + width * 2 * HK * HD),
        ),
        interpret=interpret,
    )(where, scale, doc_start, queries, *blocks, *blocks)


def body(queries, keys, values, lengths, ssmax_scale):
    tok_rows = queries.shape[0]
    slab_rows = tok_rows * lax.axis_size("grp")
    doc_most = WIN_DEV * tok_rows
    grp_index = lax.axis_index("grp")
    ctx_index = lax.axis_index("ctx")
    q_start = ctx_index * slab_rows + grp_index * tok_rows
    q_pos = q_start + jnp.arange(tok_rows, dtype=jnp.int32)
    own = jnp.concatenate([keys, values], axis=1)
    blocks = window_blocks(own)
    totals = jnp.cumsum(lengths, dtype=jnp.int32)
    before = totals[None, :] <= q_pos[:, None]
    doc_start = jnp.sum(jnp.where(before, lengths[None, :], 0), axis=1, dtype=jnp.int32)
    where = jnp.stack([q_start, grp_index % 2]).astype(jnp.int32)
    return attend(queries, blocks, where, ssmax_scale, doc_start[:, None])


def solution(mesh):
    return jax.shard_map(
        body,
        mesh=mesh,
        in_specs=(
            P(AXES, None),
            P(AXES, None),
            P(AXES, None),
            P(),
            P(),
        ),
        out_specs=P(AXES, None),
        check_vma=False,
    )
```

```python
import functools

import jax
import jax.numpy as jnp
from jax import lax
from jax.experimental import pallas as pl
from jax.experimental.pallas import tpu as pltpu
from jax.sharding import PartitionSpec as P

HQ = 32
HK = 4
HD = 128
WIN_DEV = 4
AXES = ("ctx", "grp")


def send(x, pairs):
    return lax.ppermute(x, AXES, pairs)


def far_receivers(mesh):
    flat = list(mesh.devices.reshape(-1))
    try:
        chips = [tuple(d.coords) for d in flat]
    except AttributeError:
        return ()
    sizes = [max(c[a] for c in chips) + 1 for a in range(len(chips[0]))]

    def hops(a, b):
        return sum(min(abs(p - q), n - abs(p - q)) for p, q, n in zip(a, b, sizes))

    return tuple(i for i in range(4, len(flat)) if hops(chips[i - 2], chips[i]) >= 3)


def window_blocks(own, far):
    count = lax.axis_size("ctx") * lax.axis_size("grp")
    ahead2 = [(i, i + 2) for i in range(count - 2)]
    to_odd = [(i, i + 1) for i in range(0, count - 1, 2)]
    to_even = [(i, i - 1) for i in range(1, count, 2)]
    swap = to_odd + to_even
    far_set = set(far)
    back2 = send(own, ahead2)
    from_even_own = send(own, to_odd)
    direct4 = send(own, [(i - 4, i) for i in far])
    forward2 = [(i, j) for i, j in ahead2 if j not in far_set]
    back4 = send(back2, forward2) + direct4 if far else send(back2, forward2)
    swapped2 = send(back2, swap)
    from_odd4 = send(back4, to_even)
    return [back4, from_odd4, swapped2, back2, from_even_own, own]


def attend_kernel(qs_ref, scale_ref, ds_ref, q_ref, *refs):
    kv_refs, o_ref = refs[:-1], refs[-1]
    half = len(kv_refs) // 2
    rows = q_ref.shape[0]
    width = rows * (half - 1)
    doc_most = width - rows
    head = pl.program_id(0)
    q_start = qs_ref[0]
    even = qs_ref[1] == 0

    def ordered(r):
        back4, odd4, swap2, back2, even_own, own = [x[...] for x in r]
        back3 = jnp.where(even, odd4, swap2)
        back1 = jnp.where(even, swap2, even_own)
        return jnp.concatenate([back4, back3, back2, back1, own], axis=0)

    col = lax.broadcasted_iota(jnp.int32, (rows, width), 1)
    row = lax.broadcasted_iota(jnp.int32, (rows, width), 0)
    doc_start = ds_ref[...]
    live = (col >= doc_start - (q_start - doc_most)) & (col <= row + doc_most)
    k = ordered(kv_refs[:half])
    v = ordered(kv_refs[half:])
    q_pos = q_start + lax.broadcasted_iota(jnp.int32, (rows, 1), 0)
    logv = jnp.log((q_pos - doc_start + 1).astype(jnp.float32))
    per_group = HQ // HK
    coef = jnp.stack(
        [scale_ref[head * per_group + g] * logv / jnp.sqrt(jnp.float32(HD)) for g in range(per_group)]
    )
    q = jnp.concatenate([q_ref[:, g * HD : (g + 1) * HD] for g in range(per_group)], axis=0)
    s = lax.dot_general(q, k, (((1,), (1,)), ((), ())), preferred_element_type=jnp.float32)
    s = jnp.where(live[None], s.reshape(per_group, rows, width) * coef, -jnp.inf)
    m = jnp.max(s, axis=2, keepdims=True)
    p = jnp.exp(s - m)
    l = jnp.sum(p, axis=2, keepdims=True)
    w = (p * (1.0 / l)).astype(jnp.bfloat16).reshape(per_group * rows, width)
    o = jnp.dot(w, v, preferred_element_type=jnp.float32)
    for g in range(per_group):
        o_ref[:, g * HD : (g + 1) * HD] = o[g * rows : (g + 1) * rows].astype(o_ref.dtype)


def attend(queries, blocks, where, scale, doc_start, interpret=False):
    rows = queries.shape[0]
    width = rows * (len(blocks) - 1)
    per_group = HQ // HK
    flops = 4 * HQ * rows * width * HD
    k_specs = [pl.BlockSpec((rows, HD), lambda h: (0, h)) for _ in blocks]
    v_specs = [pl.BlockSpec((rows, HD), lambda h: (0, h + HK)) for _ in blocks]
    return pl.pallas_call(
        attend_kernel,
        grid=(HK,),
        in_specs=[
            pl.BlockSpec(memory_space=pltpu.SMEM),
            pl.BlockSpec(memory_space=pltpu.SMEM),
            pl.BlockSpec((rows, 1), lambda h: (0, 0)),
            pl.BlockSpec((rows, per_group * HD), lambda h: (0, h)),
        ]
        + k_specs
        + v_specs,
        out_specs=pl.BlockSpec((rows, per_group * HD), lambda h: (0, h)),
        out_shape=jax.ShapeDtypeStruct((rows, HQ * HD), jnp.bfloat16),
        cost_estimate=pl.CostEstimate(
            flops=flops,
            transcendentals=HQ * rows * width,
            bytes_accessed=2 * (2 * rows * HQ * HD + width * 2 * HK * HD),
        ),
        interpret=interpret,
    )(where, scale, doc_start, queries, *blocks, *blocks)


def body(queries, keys, values, lengths, ssmax_scale, far=()):
    tok_rows = queries.shape[0]
    slab_rows = tok_rows * lax.axis_size("grp")
    doc_most = WIN_DEV * tok_rows
    grp_index = lax.axis_index("grp")
    ctx_index = lax.axis_index("ctx")
    q_start = ctx_index * slab_rows + grp_index * tok_rows
    q_pos = q_start + jnp.arange(tok_rows, dtype=jnp.int32)
    own = jnp.concatenate([keys, values], axis=1)
    blocks = window_blocks(own, far)
    totals = jnp.cumsum(lengths, dtype=jnp.int32)
    before = totals[None, :] <= q_pos[:, None]
    doc_start = jnp.sum(jnp.where(before, lengths[None, :], 0), axis=1, dtype=jnp.int32)
    where = jnp.stack([q_start, grp_index % 2]).astype(jnp.int32)
    return attend(queries, blocks, where, ssmax_scale, doc_start[:, None])


def solution(mesh):
    return jax.shard_map(
        functools.partial(body, far=far_receivers(mesh)),
        mesh=mesh,
        in_specs=(
            P(AXES, None),
            P(AXES, None),
            P(AXES, None),
            P(),
            P(),
        ),
        out_specs=P(AXES, None),
        check_vma=False,
    )
```

```python
import functools

import jax
import jax.numpy as jnp
from jax import lax
from jax.experimental import pallas as pl
from jax.experimental.pallas import tpu as pltpu
from jax.sharding import PartitionSpec as P

HQ = 32
HK = 4
HD = 128
WIN_DEV = 4
AXES = ("ctx", "grp")


def send(x, pairs):
    return lax.ppermute(x, AXES, pairs)


def far_receivers(mesh):
    flat = list(mesh.devices.reshape(-1))
    try:
        chips = [tuple(d.coords) for d in flat]
    except AttributeError:
        return ()
    sizes = [max(c[a] for c in chips) + 1 for a in range(len(chips[0]))]

    def hops(a, b):
        return sum(min(abs(p - q), n - abs(p - q)) for p, q, n in zip(a, b, sizes))

    return tuple(i for i in range(4, len(flat)) if hops(chips[i - 4], chips[i]) >= 3)


def window_blocks(own, far):
    count = lax.axis_size("ctx") * lax.axis_size("grp")
    ahead2 = [(i, i + 2) for i in range(count - 2)]
    to_odd = [(i, i + 1) for i in range(0, count - 1, 2)]
    to_even = [(i, i - 1) for i in range(1, count, 2)]
    swap = to_odd + to_even
    far_set = set(far)
    back2 = send(own, ahead2)
    from_even_own = send(own, to_odd)
    direct4 = send(own, [(i - 4, i) for i in far])
    forward2 = [(i, j) for i, j in ahead2 if j not in far_set]
    back4 = send(back2, forward2) + direct4 if far else send(back2, forward2)
    swapped2 = send(back2, swap)
    from_odd4 = send(back4, to_even)
    return [back4, from_odd4, swapped2, back2, from_even_own, own]


def attend_kernel(qs_ref, scale_ref, ds_ref, q_ref, *refs):
    kv_refs, o_ref = refs[:-1], refs[-1]
    half = len(kv_refs) // 2
    rows = q_ref.shape[0]
    width = rows * (half - 1)
    doc_most = width - rows
    head = pl.program_id(0)
    q_start = qs_ref[0]
    even = qs_ref[1] == 0

    def ordered(r):
        back4, odd4, swap2, back2, even_own, own = [x[...] for x in r]
        back3 = jnp.where(even, odd4, swap2)
        back1 = jnp.where(even, swap2, even_own)
        return jnp.concatenate([back4, back3, back2, back1, own], axis=0)

    col = lax.broadcasted_iota(jnp.int32, (rows, width), 1)
    row = lax.broadcasted_iota(jnp.int32, (rows, width), 0)
    doc_start = ds_ref[...]
    live = (col >= doc_start - (q_start - doc_most)) & (col <= row + doc_most)
    k = ordered(kv_refs[:half])
    v = ordered(kv_refs[half:])
    q_pos = q_start + lax.broadcasted_iota(jnp.int32, (rows, 1), 0)
    logv = jnp.log((q_pos - doc_start + 1).astype(jnp.float32))
    per_group = HQ // HK
    coef = jnp.stack(
        [scale_ref[head * per_group + g] * logv / jnp.sqrt(jnp.float32(HD)) for g in range(per_group)]
    )
    q = jnp.concatenate([q_ref[:, g * HD : (g + 1) * HD] for g in range(per_group)], axis=0)
    s = lax.dot_general(q, k, (((1,), (1,)), ((), ())), preferred_element_type=jnp.float32)
    s = jnp.where(live[None], s.reshape(per_group, rows, width) * coef, -jnp.inf)
    m = jnp.max(s, axis=2, keepdims=True)
    p = jnp.exp(s - m)
    l = jnp.sum(p, axis=2, keepdims=True)
    w = (p * (1.0 / l)).astype(jnp.bfloat16).reshape(per_group * rows, width)
    o = jnp.dot(w, v, preferred_element_type=jnp.float32)
    for g in range(per_group):
        o_ref[:, g * HD : (g + 1) * HD] = o[g * rows : (g + 1) * rows].astype(o_ref.dtype)


def attend(queries, blocks, where, scale, doc_start, interpret=False):
    rows = queries.shape[0]
    width = rows * (len(blocks) - 1)
    per_group = HQ // HK
    flops = 4 * HQ * rows * width * HD
    k_specs = [pl.BlockSpec((rows, HD), lambda h: (0, h)) for _ in blocks]
    v_specs = [pl.BlockSpec((rows, HD), lambda h: (0, h + HK)) for _ in blocks]
    return pl.pallas_call(
        attend_kernel,
        grid=(HK,),
        in_specs=[
            pl.BlockSpec(memory_space=pltpu.SMEM),
            pl.BlockSpec(memory_space=pltpu.SMEM),
            pl.BlockSpec((rows, 1), lambda h: (0, 0)),
            pl.BlockSpec((rows, per_group * HD), lambda h: (0, h)),
        ]
        + k_specs
        + v_specs,
        out_specs=pl.BlockSpec((rows, per_group * HD), lambda h: (0, h)),
        out_shape=jax.ShapeDtypeStruct((rows, HQ * HD), jnp.bfloat16),
        cost_estimate=pl.CostEstimate(
            flops=flops,
            transcendentals=HQ * rows * width,
            bytes_accessed=2 * (2 * rows * HQ * HD + width * 2 * HK * HD),
        ),
        interpret=interpret,
    )(where, scale, doc_start, queries, *blocks, *blocks)


def body(queries, keys, values, lengths, ssmax_scale, far=()):
    tok_rows = queries.shape[0]
    slab_rows = tok_rows * lax.axis_size("grp")
    doc_most = WIN_DEV * tok_rows
    grp_index = lax.axis_index("grp")
    ctx_index = lax.axis_index("ctx")
    q_start = ctx_index * slab_rows + grp_index * tok_rows
    q_pos = q_start + jnp.arange(tok_rows, dtype=jnp.int32)
    own = jnp.concatenate([keys, values], axis=1)
    blocks = window_blocks(own, far)
    totals = jnp.cumsum(lengths, dtype=jnp.int32)
    before = totals[None, :] <= q_pos[:, None]
    doc_start = jnp.sum(jnp.where(before, lengths[None, :], 0), axis=1, dtype=jnp.int32)
    where = jnp.stack([q_start, grp_index % 2]).astype(jnp.int32)
    return attend(queries, blocks, where, ssmax_scale, doc_start[:, None])


def solution(mesh):
    return jax.shard_map(
        functools.partial(body, far=far_receivers(mesh)),
        mesh=mesh,
        in_specs=(
            P(AXES, None),
            P(AXES, None),
            P(AXES, None),
            P(),
            P(),
        ),
        out_specs=P(AXES, None),
        check_vma=False,
    )
```

```python
import functools

import jax
import jax.numpy as jnp
from jax import lax
from jax.experimental import pallas as pl
from jax.experimental.pallas import tpu as pltpu
from jax.sharding import PartitionSpec as P

HQ = 32
HK = 4
HD = 128
WIN_DEV = 4
CHUNK = 16
AXES = ("ctx", "grp")


def send(x, pairs):
    return lax.ppermute(x, AXES, pairs)


def far_receivers(mesh):
    flat = list(mesh.devices.reshape(-1))
    try:
        chips = [tuple(d.coords) for d in flat]
    except AttributeError:
        return ()
    sizes = [max(c[a] for c in chips) + 1 for a in range(len(chips[0]))]

    def hops(a, b):
        return sum(min(abs(p - q), n - abs(p - q)) for p, q, n in zip(a, b, sizes))

    return tuple(i for i in range(4, len(flat)) if hops(chips[i - 2], chips[i]) >= 3)


def window_blocks(own, far):
    count = lax.axis_size("ctx") * lax.axis_size("grp")
    ahead2 = [(i, i + 2) for i in range(count - 2)]
    to_odd = [(i, i + 1) for i in range(0, count - 1, 2)]
    to_even = [(i, i - 1) for i in range(1, count, 2)]
    swap = to_odd + to_even
    far_set = set(far)
    back2 = send(own, ahead2)
    from_even_own = send(own, to_odd)
    direct4 = send(own, [(i - 4, i) for i in far])
    forward2 = [(i, j) for i, j in ahead2 if j not in far_set]
    back4 = send(back2, forward2) + direct4 if far else send(back2, forward2)
    swapped2 = send(back2, swap)
    from_odd4 = send(back4, to_even)
    return [back4, from_odd4, swapped2, back2, from_even_own, own]


def attend_kernel(qs_ref, scale_ref, ds_ref, q_ref, *refs):
    kv_refs, o_ref = refs[:-5], refs[-5]
    s_ref, w_ref, coef_ref, lo_ref = refs[-4:]
    half = len(kv_refs) // 2
    rows = q_ref.shape[0]
    width = rows * (half - 1)
    doc_most = width - rows
    head = pl.program_id(0)
    q_start = qs_ref[0]
    even = qs_ref[1] == 0

    def ordered(r):
        back4, odd4, swap2, back2, even_own, own = [x[...] for x in r]
        back3 = jnp.where(even, odd4, swap2)
        back1 = jnp.where(even, swap2, even_own)
        return jnp.concatenate([back4, back3, back2, back1, own], axis=0)

    doc_start = ds_ref[...]
    k = ordered(kv_refs[:half])
    v = ordered(kv_refs[half:])
    q_pos = q_start + lax.broadcasted_iota(jnp.int32, (rows, 1), 0)
    logv = jnp.log((q_pos - doc_start + 1).astype(jnp.float32))
    per_group = HQ // HK
    for g in range(per_group):
        coef_ref[g * rows : (g + 1) * rows, :] = scale_ref[head * per_group + g] * logv / jnp.sqrt(jnp.float32(HD))
    lo_ref[...] = doc_start - (q_start - doc_most)
    q = jnp.concatenate([q_ref[:, g * HD : (g + 1) * HD] for g in range(per_group)], axis=0)
    s_ref[...] = lax.dot_general(q, k, (((1,), (1,)), ((), ())), preferred_element_type=jnp.float32)

    def chunk(c, carry):
        r0 = pl.multiple_of(c * CHUNK, CHUNK)
        i0 = pl.multiple_of((c % (rows // CHUNK)) * CHUNK, CHUNK)
        col = lax.broadcasted_iota(jnp.int32, (CHUNK, width), 1)
        row = lax.broadcasted_iota(jnp.int32, (CHUNK, width), 0) + i0
        live = (col >= lo_ref[pl.ds(i0, CHUNK), :]) & (col <= row + doc_most)
        x = jnp.where(live, s_ref[pl.ds(r0, CHUNK), :] * coef_ref[pl.ds(r0, CHUNK), :], -jnp.inf)
        m = jnp.max(x, axis=1, keepdims=True)
        p = jnp.exp(x - m)
        l = jnp.sum(p, axis=1, keepdims=True)
        w_ref[pl.ds(r0, CHUNK), :] = (p * (1.0 / l)).astype(jnp.bfloat16)
        return carry

    lax.fori_loop(0, per_group * rows // CHUNK, chunk, 0, unroll=2)
    o = jnp.dot(w_ref[...], v, preferred_element_type=jnp.float32)
    for g in range(per_group):
        o_ref[:, g * HD : (g + 1) * HD] = o[g * rows : (g + 1) * rows].astype(o_ref.dtype)

def attend(queries, blocks, where, scale, doc_start, interpret=False):
    rows = queries.shape[0]
    width = rows * (len(blocks) - 1)
    per_group = HQ // HK
    flops = 4 * HQ * rows * width * HD
    k_specs = [pl.BlockSpec((rows, HD), lambda h: (0, h)) for _ in blocks]
    v_specs = [pl.BlockSpec((rows, HD), lambda h: (0, h + HK)) for _ in blocks]
    return pl.pallas_call(
        attend_kernel,
        grid=(HK,),
        in_specs=[
            pl.BlockSpec(memory_space=pltpu.SMEM),
            pl.BlockSpec(memory_space=pltpu.SMEM),
            pl.BlockSpec((rows, 1), lambda h: (0, 0)),
            pl.BlockSpec((rows, per_group * HD), lambda h: (0, h)),
        ]
        + k_specs
        + v_specs,
        out_specs=pl.BlockSpec((rows, per_group * HD), lambda h: (0, h)),
        out_shape=jax.ShapeDtypeStruct((rows, HQ * HD), jnp.bfloat16),
        scratch_shapes=[
            pltpu.VMEM((per_group * rows, width), jnp.float32),
            pltpu.VMEM((per_group * rows, width), jnp.bfloat16),
            pltpu.VMEM((per_group * rows, 1), jnp.float32),
            pltpu.VMEM((rows, 1), jnp.int32),
        ],
        cost_estimate=pl.CostEstimate(
            flops=flops,
            transcendentals=HQ * rows * width,
            bytes_accessed=2 * (2 * rows * HQ * HD + width * 2 * HK * HD),
        ),
        interpret=interpret,
    )(where, scale, doc_start, queries, *blocks, *blocks)


def body(queries, keys, values, lengths, ssmax_scale, far=()):
    tok_rows = queries.shape[0]
    slab_rows = tok_rows * lax.axis_size("grp")
    doc_most = WIN_DEV * tok_rows
    grp_index = lax.axis_index("grp")
    ctx_index = lax.axis_index("ctx")
    q_start = ctx_index * slab_rows + grp_index * tok_rows
    q_pos = q_start + jnp.arange(tok_rows, dtype=jnp.int32)
    own = jnp.concatenate([keys, values], axis=1)
    blocks = window_blocks(own, far)
    totals = jnp.cumsum(lengths, dtype=jnp.int32)
    before = totals[None, :] <= q_pos[:, None]
    doc_start = jnp.sum(jnp.where(before, lengths[None, :], 0), axis=1, dtype=jnp.int32)
    where = jnp.stack([q_start, grp_index % 2]).astype(jnp.int32)
    return attend(queries, blocks, where, ssmax_scale, doc_start[:, None])


def solution(mesh):
    return jax.shard_map(
        functools.partial(body, far=far_receivers(mesh)),
        mesh=mesh,
        in_specs=(
            P(AXES, None),
            P(AXES, None),
            P(AXES, None),
            P(),
            P(),
        ),
        out_specs=P(AXES, None),
        check_vma=False,
    )
```

```python
import functools

import jax
import jax.numpy as jnp
from jax import lax
from jax.experimental import pallas as pl
from jax.experimental.pallas import tpu as pltpu
from jax.sharding import PartitionSpec as P

HQ = 32
HK = 4
HD = 128
WIN_DEV = 4
AXES = ("ctx", "grp")


def send(x, pairs):
    return lax.ppermute(x, AXES, pairs)


def far_receivers(mesh):
    flat = list(mesh.devices.reshape(-1))
    try:
        chips = [tuple(d.coords) for d in flat]
    except AttributeError:
        return ()
    sizes = [max(c[a] for c in chips) + 1 for a in range(len(chips[0]))]

    def hops(a, b):
        return sum(min(abs(p - q), n - abs(p - q)) for p, q, n in zip(a, b, sizes))

    return tuple(i for i in range(4, len(flat)) if hops(chips[i - 2], chips[i]) >= 3)


def window_blocks(own, far, early):
    count = lax.axis_size("ctx") * lax.axis_size("grp")
    ahead2 = [(i, i + 2) for i in range(count - 2)]
    to_odd = [(i, i + 1) for i in range(0, count - 1, 2)]
    to_even = [(i, i - 1) for i in range(1, count, 2)]
    swap = to_odd + to_even
    far_set = set(far)
    back2 = send(own, ahead2)
    back2, early = lax.optimization_barrier((back2, early))
    from_even_own = send(own, to_odd)
    direct4 = send(own, [(i - 4, i) for i in far])
    forward2 = [(i, j) for i, j in ahead2 if j not in far_set]
    back4 = send(back2, forward2) + direct4 if far else send(back2, forward2)
    swapped2 = send(back2, swap)
    from_odd4 = send(back4, to_even)
    return [back4, from_odd4, swapped2, back2, from_even_own, own], early


def attend_kernel(qs_ref, scale_ref, ds_ref, q_ref, *refs):
    kv_refs, o_ref = refs[:-1], refs[-1]
    half = len(kv_refs) // 2
    rows = q_ref.shape[0]
    width = rows * (half - 1)
    doc_most = width - rows
    head = pl.program_id(0)
    q_start = qs_ref[0]
    even = qs_ref[1] == 0

    def ordered(r):
        back4, odd4, swap2, back2, even_own, own = [x[...] for x in r]
        back3 = jnp.where(even, odd4, swap2)
        back1 = jnp.where(even, swap2, even_own)
        return jnp.concatenate([back4, back3, back2, back1, own], axis=0)

    col = lax.broadcasted_iota(jnp.int32, (rows, width), 1)
    row = lax.broadcasted_iota(jnp.int32, (rows, width), 0)
    doc_start = ds_ref[...]
    live = (col >= doc_start - (q_start - doc_most)) & (col <= row + doc_most)
    k = ordered(kv_refs[:half])
    v = ordered(kv_refs[half:])
    q_pos = q_start + lax.broadcasted_iota(jnp.int32, (rows, 1), 0)
    logv = jnp.log((q_pos - doc_start + 1).astype(jnp.float32))
    per_group = HQ // HK
    coef = jnp.stack(
        [scale_ref[head * per_group + g] * logv / jnp.sqrt(jnp.float32(HD)) for g in range(per_group)]
    )
    q = jnp.concatenate([q_ref[:, g * HD : (g + 1) * HD] for g in range(per_group)], axis=0)
    s = lax.dot_general(q, k, (((1,), (1,)), ((), ())), preferred_element_type=jnp.float32)
    s = jnp.where(live[None], s.reshape(per_group, rows, width) * coef, -jnp.inf)
    m = jnp.max(s, axis=2, keepdims=True)
    p = jnp.exp(s - m)
    l = jnp.sum(p, axis=2, keepdims=True)
    w = (p * (1.0 / l)).astype(jnp.bfloat16).reshape(per_group * rows, width)
    o = jnp.dot(w, v, preferred_element_type=jnp.float32)
    for g in range(per_group):
        o_ref[:, g * HD : (g + 1) * HD] = o[g * rows : (g + 1) * rows].astype(o_ref.dtype)


def attend(queries, blocks, where, scale, doc_start, interpret=False):
    rows = queries.shape[0]
    width = rows * (len(blocks) - 1)
    per_group = HQ // HK
    flops = 4 * HQ * rows * width * HD
    k_specs = [pl.BlockSpec((rows, HD), lambda h: (0, h)) for _ in blocks]
    v_specs = [pl.BlockSpec((rows, HD), lambda h: (0, h + HK)) for _ in blocks]
    return pl.pallas_call(
        attend_kernel,
        grid=(HK,),
        in_specs=[
            pl.BlockSpec(memory_space=pltpu.SMEM),
            pl.BlockSpec(memory_space=pltpu.SMEM),
            pl.BlockSpec((rows, 1), lambda h: (0, 0)),
            pl.BlockSpec((rows, per_group * HD), lambda h: (0, h)),
        ]
        + k_specs
        + v_specs,
        out_specs=pl.BlockSpec((rows, per_group * HD), lambda h: (0, h)),
        out_shape=jax.ShapeDtypeStruct((rows, HQ * HD), jnp.bfloat16),
        cost_estimate=pl.CostEstimate(
            flops=flops,
            transcendentals=HQ * rows * width,
            bytes_accessed=2 * (2 * rows * HQ * HD + width * 2 * HK * HD),
        ),
        interpret=interpret,
    )(where, scale, doc_start, queries, *blocks, *blocks)


def body(queries, keys, values, lengths, ssmax_scale, far=()):
    tok_rows = queries.shape[0]
    slab_rows = tok_rows * lax.axis_size("grp")
    doc_most = WIN_DEV * tok_rows
    grp_index = lax.axis_index("grp")
    ctx_index = lax.axis_index("ctx")
    q_start = ctx_index * slab_rows + grp_index * tok_rows
    q_pos = q_start + jnp.arange(tok_rows, dtype=jnp.int32)
    own = jnp.concatenate([keys, values], axis=1)
    totals = jnp.cumsum(lengths, dtype=jnp.int32)
    before = totals[None, :] <= q_pos[:, None]
    doc_start = jnp.sum(jnp.where(before, lengths[None, :], 0), axis=1, keepdims=True, dtype=jnp.int32)
    where = jnp.stack([q_start, grp_index % 2]).astype(jnp.int32)
    blocks, (where, doc_start) = window_blocks(own, far, (where, doc_start))
    return attend(queries, blocks, where, ssmax_scale, doc_start)


def solution(mesh):
    return jax.shard_map(
        functools.partial(body, far=far_receivers(mesh)),
        mesh=mesh,
        in_specs=(
            P(AXES, None),
            P(AXES, None),
            P(AXES, None),
            P(),
            P(),
        ),
        out_specs=P(AXES, None),
        check_vma=False,
    )
```

```python
import functools

import jax
import jax.numpy as jnp
from jax import lax
from jax.experimental import pallas as pl
from jax.experimental.pallas import tpu as pltpu
from jax.sharding import PartitionSpec as P

HQ = 32
HK = 4
HD = 128
WIN_DEV = 4
AXES = ("ctx", "grp")


def send(x, pairs):
    return lax.ppermute(x, AXES, pairs)


def far_receivers(mesh):
    flat = list(mesh.devices.reshape(-1))
    try:
        chips = [tuple(d.coords) for d in flat]
    except AttributeError:
        return ()
    sizes = [max(c[a] for c in chips) + 1 for a in range(len(chips[0]))]

    def hops(a, b):
        return sum(min(abs(p - q), n - abs(p - q)) for p, q, n in zip(a, b, sizes))

    return tuple(i for i in range(4, len(flat)) if hops(chips[i - 2], chips[i]) >= 3)


def window_blocks(own, far):
    count = lax.axis_size("ctx") * lax.axis_size("grp")
    ahead2 = [(i, i + 2) for i in range(count - 2)]
    to_odd = [(i, i + 1) for i in range(0, count - 1, 2)]
    to_even = [(i, i - 1) for i in range(1, count, 2)]
    swap = to_odd + to_even
    far_set = set(far)
    back2 = send(own, ahead2)
    from_even_own = send(own, to_odd)
    direct4 = send(own, [(i - 4, i) for i in far])
    forward2 = [(i, j) for i, j in ahead2 if j not in far_set]
    forward4 = send(back2, forward2)
    swapped2 = send(back2, swap)
    odd_to_next = [(i, i + 1) for i in range(1, count - 1, 2) if i + 1 not in far_set]
    from_prev_odd = send(back2, odd_to_next)
    from_odd_direct = send(direct4, [(i, i - 1) for i in far if i % 2 == 1])
    return [forward4, direct4, from_prev_odd, from_odd_direct, swapped2, back2, from_even_own, own]


def attend_kernel(qs_ref, scale_ref, ds_ref, q_ref, *refs):
    kv_refs, o_ref = refs[:-1], refs[-1]
    half = len(kv_refs) // 2
    rows = q_ref.shape[0]
    width = rows * (half - 3)
    doc_most = width - rows
    head = pl.program_id(0)
    q_start = qs_ref[0]
    even = qs_ref[1] == 0

    def ordered(r):
        fwd4, direct4, prev_odd, odd_direct, swap2, back2, even_own, own = [x[...] for x in r]
        back4 = fwd4 + direct4
        back3 = jnp.where(even, prev_odd + odd_direct, swap2)
        back1 = jnp.where(even, swap2, even_own)
        return jnp.concatenate([back4, back3, back2, back1, own], axis=0)

    col = lax.broadcasted_iota(jnp.int32, (rows, width), 1)
    row = lax.broadcasted_iota(jnp.int32, (rows, width), 0)
    doc_start = ds_ref[...]
    live = (col >= doc_start - (q_start - doc_most)) & (col <= row + doc_most)
    k = ordered(kv_refs[:half])
    v = ordered(kv_refs[half:])
    q_pos = q_start + lax.broadcasted_iota(jnp.int32, (rows, 1), 0)
    logv = jnp.log((q_pos - doc_start + 1).astype(jnp.float32))
    per_group = HQ // HK
    coef = jnp.stack(
        [scale_ref[head * per_group + g] * logv / jnp.sqrt(jnp.float32(HD)) for g in range(per_group)]
    )
    q = jnp.concatenate([q_ref[:, g * HD : (g + 1) * HD] for g in range(per_group)], axis=0)
    s = lax.dot_general(q, k, (((1,), (1,)), ((), ())), preferred_element_type=jnp.float32)
    s = jnp.where(live[None], s.reshape(per_group, rows, width) * coef, -jnp.inf)
    m = jnp.max(s, axis=2, keepdims=True)
    p = jnp.exp(s - m)
    l = jnp.sum(p, axis=2, keepdims=True)
    w = (p * (1.0 / l)).astype(jnp.bfloat16).reshape(per_group * rows, width)
    o = jnp.dot(w, v, preferred_element_type=jnp.float32)
    for g in range(per_group):
        o_ref[:, g * HD : (g + 1) * HD] = o[g * rows : (g + 1) * rows].astype(o_ref.dtype)


def attend(queries, blocks, where, scale, doc_start, interpret=False):
    rows = queries.shape[0]
    width = rows * (len(blocks) - 3)
    per_group = HQ // HK
    flops = 4 * HQ * rows * width * HD
    k_specs = [pl.BlockSpec((rows, HD), lambda h: (0, h)) for _ in blocks]
    v_specs = [pl.BlockSpec((rows, HD), lambda h: (0, h + HK)) for _ in blocks]
    return pl.pallas_call(
        attend_kernel,
        grid=(HK,),
        in_specs=[
            pl.BlockSpec(memory_space=pltpu.SMEM),
            pl.BlockSpec(memory_space=pltpu.SMEM),
            pl.BlockSpec((rows, 1), lambda h: (0, 0)),
            pl.BlockSpec((rows, per_group * HD), lambda h: (0, h)),
        ]
        + k_specs
        + v_specs,
        out_specs=pl.BlockSpec((rows, per_group * HD), lambda h: (0, h)),
        out_shape=jax.ShapeDtypeStruct((rows, HQ * HD), jnp.bfloat16),
        cost_estimate=pl.CostEstimate(
            flops=flops,
            transcendentals=HQ * rows * width,
            bytes_accessed=2 * (2 * rows * HQ * HD + width * 2 * HK * HD),
        ),
        interpret=interpret,
    )(where, scale, doc_start, queries, *blocks, *blocks)


def body(queries, keys, values, lengths, ssmax_scale, far=()):
    tok_rows = queries.shape[0]
    slab_rows = tok_rows * lax.axis_size("grp")
    doc_most = WIN_DEV * tok_rows
    grp_index = lax.axis_index("grp")
    ctx_index = lax.axis_index("ctx")
    q_start = ctx_index * slab_rows + grp_index * tok_rows
    q_pos = q_start + jnp.arange(tok_rows, dtype=jnp.int32)
    own = jnp.concatenate([keys, values], axis=1)
    blocks = window_blocks(own, far)
    totals = jnp.cumsum(lengths, dtype=jnp.int32)
    before = totals[None, :] <= q_pos[:, None]
    doc_start = jnp.sum(jnp.where(before, lengths[None, :], 0), axis=1, dtype=jnp.int32)
    where = jnp.stack([q_start, grp_index % 2]).astype(jnp.int32)
    return attend(queries, blocks, where, ssmax_scale, doc_start[:, None])


def solution(mesh):
    return jax.shard_map(
        functools.partial(body, far=far_receivers(mesh)),
        mesh=mesh,
        in_specs=(
            P(AXES, None),
            P(AXES, None),
            P(AXES, None),
            P(),
            P(),
        ),
        out_specs=P(AXES, None),
        check_vma=False,
    )
```

```python
import functools

import jax
import jax.numpy as jnp
from jax import lax
from jax.experimental import pallas as pl
from jax.experimental.pallas import tpu as pltpu
from jax.sharding import PartitionSpec as P

HQ = 32
HK = 4
HD = 128
WIN_DEV = 4
AXES = ("ctx", "grp")


def send(x, pairs):
    return lax.ppermute(x, AXES, pairs)


def far_receivers(mesh):
    flat = list(mesh.devices.reshape(-1))
    try:
        chips = [tuple(d.coords) for d in flat]
    except AttributeError:
        return ()
    sizes = [max(c[a] for c in chips) + 1 for a in range(len(chips[0]))]

    def hops(a, b):
        return sum(min(abs(p - q), n - abs(p - q)) for p, q, n in zip(a, b, sizes))

    return tuple(i for i in range(4, len(flat)) if hops(chips[i - 2], chips[i]) >= 3)


def window_blocks(own, far):
    count = lax.axis_size("ctx") * lax.axis_size("grp")
    ahead2 = [(i, i + 2) for i in range(count - 2)]
    to_odd = [(i, i + 1) for i in range(0, count - 1, 2)]
    to_even = [(i, i - 1) for i in range(1, count, 2)]
    swap = to_odd + to_even
    far_set = set(far)
    back2 = send(own, ahead2)
    from_even_own = send(own, to_odd)
    direct4 = send(own, [(i - 4, i) for i in far])
    forward2 = [(i, j) for i, j in ahead2 if j not in far_set]
    back4 = send(back2, forward2) + direct4 if far else send(back2, forward2)
    swapped2 = send(back2, swap)
    from_odd4 = send(back4, to_even)
    return [back4, from_odd4, swapped2, back2, from_even_own, own]


def attend_kernel(qs_ref, scale_ref, ds_ref, q_ref, *refs):
    kv_refs, o_ref = refs[:-1], refs[-1]
    half = len(kv_refs) // 2
    rows = q_ref.shape[0]
    width = rows * (half - 1)
    doc_most = width - rows
    head = pl.program_id(0)
    q_start = qs_ref[0]
    even = qs_ref[1] == 0

    def ordered(r):
        back4, odd4, swap2, back2, even_own, own = [x[...] for x in r]
        back3 = jnp.where(even, odd4, swap2)
        back1 = jnp.where(even, swap2, even_own)
        return jnp.concatenate([back4, back3, back2, back1, own], axis=0)

    doc_start = ds_ref[...]
    k_all = ordered(kv_refs[:half])
    v_all = ordered(kv_refs[half:])
    q_pos = q_start + lax.broadcasted_iota(jnp.int32, (rows, 1), 0)
    logv = jnp.log((q_pos - doc_start + 1).astype(jnp.float32))
    per_group = HQ // HK
    coef = jnp.stack(
        [scale_ref[head * per_group + g] * logv / jnp.sqrt(jnp.float32(HD)) for g in range(per_group)]
    )
    q = jnp.concatenate([q_ref[:, g * HD : (g + 1) * HD] for g in range(per_group)], axis=0)
    lo = doc_start - (q_start - doc_most)

    def compute(skip):
        first = skip * rows
        span = width - first
        k = k_all[first:]
        v = v_all[first:]
        col = lax.broadcasted_iota(jnp.int32, (rows, span), 1) + first
        row = lax.broadcasted_iota(jnp.int32, (rows, span), 0)
        live = (col >= lo) & (col <= row + doc_most)
        s = lax.dot_general(q, k, (((1,), (1,)), ((), ())), preferred_element_type=jnp.float32)
        s = jnp.where(live[None], s.reshape(per_group, rows, span) * coef, -jnp.inf)
        m = jnp.max(s, axis=2, keepdims=True)
        p = jnp.exp(s - m)
        l = jnp.sum(p, axis=2, keepdims=True)
        w = (p * (1.0 / l)).astype(jnp.bfloat16).reshape(per_group * rows, span)
        o = jnp.dot(w, v, preferred_element_type=jnp.float32)
        for g in range(per_group):
            o_ref[:, g * HD : (g + 1) * HD] = o[g * rows : (g + 1) * rows].astype(o_ref.dtype)

    for skip in range(half - 1):
        pl.when(qs_ref[2] == skip)(functools.partial(compute, skip))

def attend(queries, blocks, where, scale, doc_start, interpret=False):
    rows = queries.shape[0]
    width = rows * (len(blocks) - 1)
    per_group = HQ // HK
    flops = 4 * HQ * rows * width * HD
    k_specs = [pl.BlockSpec((rows, HD), lambda h: (0, h)) for _ in blocks]
    v_specs = [pl.BlockSpec((rows, HD), lambda h: (0, h + HK)) for _ in blocks]
    return pl.pallas_call(
        attend_kernel,
        grid=(HK,),
        in_specs=[
            pl.BlockSpec(memory_space=pltpu.SMEM),
            pl.BlockSpec(memory_space=pltpu.SMEM),
            pl.BlockSpec((rows, 1), lambda h: (0, 0)),
            pl.BlockSpec((rows, per_group * HD), lambda h: (0, h)),
        ]
        + k_specs
        + v_specs,
        out_specs=pl.BlockSpec((rows, per_group * HD), lambda h: (0, h)),
        out_shape=jax.ShapeDtypeStruct((rows, HQ * HD), jnp.bfloat16),
        cost_estimate=pl.CostEstimate(
            flops=flops,
            transcendentals=HQ * rows * width,
            bytes_accessed=2 * (2 * rows * HQ * HD + width * 2 * HK * HD),
        ),
        interpret=interpret,
    )(where, scale, doc_start, queries, *blocks, *blocks)


def body(queries, keys, values, lengths, ssmax_scale, far=()):
    tok_rows = queries.shape[0]
    slab_rows = tok_rows * lax.axis_size("grp")
    doc_most = WIN_DEV * tok_rows
    grp_index = lax.axis_index("grp")
    ctx_index = lax.axis_index("ctx")
    q_start = ctx_index * slab_rows + grp_index * tok_rows
    q_pos = q_start + jnp.arange(tok_rows, dtype=jnp.int32)
    own = jnp.concatenate([keys, values], axis=1)
    blocks = window_blocks(own, far)
    totals = jnp.cumsum(lengths, dtype=jnp.int32)
    before = totals[None, :] <= q_pos[:, None]
    doc_start = jnp.sum(jnp.where(before, lengths[None, :], 0), axis=1, dtype=jnp.int32)
    skip = jnp.clip((doc_start[0] - (q_start - doc_most)) // tok_rows, 0, WIN_DEV)
    where = jnp.stack([q_start, grp_index % 2, skip]).astype(jnp.int32)
    return attend(queries, blocks, where, ssmax_scale, doc_start[:, None])


def solution(mesh):
    return jax.shard_map(
        functools.partial(body, far=far_receivers(mesh)),
        mesh=mesh,
        in_specs=(
            P(AXES, None),
            P(AXES, None),
            P(AXES, None),
            P(),
            P(),
        ),
        out_specs=P(AXES, None),
        check_vma=False,
    )
```

```python
import functools

import jax
import jax.numpy as jnp
from jax import lax
from jax.experimental import pallas as pl
from jax.experimental.pallas import tpu as pltpu
from jax.sharding import PartitionSpec as P

HQ = 32
HK = 4
HD = 128
WIN_DEV = 4
AXES = ("ctx", "grp")


def send(x, pairs):
    return lax.ppermute(x, AXES, pairs)


def far_receivers(mesh):
    flat = list(mesh.devices.reshape(-1))
    try:
        chips = [tuple(d.coords) for d in flat]
    except AttributeError:
        return ()
    sizes = [max(c[a] for c in chips) + 1 for a in range(len(chips[0]))]

    def hops(a, b):
        return sum(min(abs(p - q), n - abs(p - q)) for p, q, n in zip(a, b, sizes))

    return tuple(i for i in range(4, len(flat)) if hops(chips[i - 4], chips[i]) >= 3 and chips[i - 4][0] != chips[i][0])


def window_blocks(own, far):
    count = lax.axis_size("ctx") * lax.axis_size("grp")
    ahead2 = [(i, i + 2) for i in range(count - 2)]
    to_odd = [(i, i + 1) for i in range(0, count - 1, 2)]
    to_even = [(i, i - 1) for i in range(1, count, 2)]
    swap = to_odd + to_even
    far_set = set(far)
    back2 = send(own, ahead2)
    from_even_own = send(own, to_odd)
    direct4 = send(own, [(i - 4, i) for i in far])
    forward2 = [(i, j) for i, j in ahead2 if j not in far_set]
    back4 = send(back2, forward2) + direct4 if far else send(back2, forward2)
    swapped2 = send(back2, swap)
    from_odd4 = send(back4, to_even)
    return [back4, from_odd4, swapped2, back2, from_even_own, own]


def attend_kernel(qs_ref, scale_ref, ds_ref, q_ref, *refs):
    kv_refs, o_ref = refs[:-1], refs[-1]
    half = len(kv_refs) // 2
    rows = q_ref.shape[0]
    width = rows * (half - 1)
    doc_most = width - rows
    head = pl.program_id(0)
    q_start = qs_ref[0]
    even = qs_ref[1] == 0

    def ordered(r):
        back4, odd4, swap2, back2, even_own, own = [x[...] for x in r]
        back3 = jnp.where(even, odd4, swap2)
        back1 = jnp.where(even, swap2, even_own)
        return jnp.concatenate([back4, back3, back2, back1, own], axis=0)

    col = lax.broadcasted_iota(jnp.int32, (rows, width), 1)
    row = lax.broadcasted_iota(jnp.int32, (rows, width), 0)
    doc_start = ds_ref[...]
    live = (col >= doc_start - (q_start - doc_most)) & (col <= row + doc_most)
    k = ordered(kv_refs[:half])
    v = ordered(kv_refs[half:])
    q_pos = q_start + lax.broadcasted_iota(jnp.int32, (rows, 1), 0)
    logv = jnp.log((q_pos - doc_start + 1).astype(jnp.float32))
    per_group = HQ // HK
    coef = jnp.stack(
        [scale_ref[head * per_group + g] * logv / jnp.sqrt(jnp.float32(HD)) for g in range(per_group)]
    )
    q = jnp.concatenate([q_ref[:, g * HD : (g + 1) * HD] for g in range(per_group)], axis=0)
    s = lax.dot_general(q, k, (((1,), (1,)), ((), ())), preferred_element_type=jnp.float32)
    s = jnp.where(live[None], s.reshape(per_group, rows, width) * coef, -jnp.inf)
    m = jnp.max(s, axis=2, keepdims=True)
    p = jnp.exp(s - m)
    l = jnp.sum(p, axis=2, keepdims=True)
    w = (p * (1.0 / l)).astype(jnp.bfloat16).reshape(per_group * rows, width)
    o = jnp.dot(w, v, preferred_element_type=jnp.float32)
    for g in range(per_group):
        o_ref[:, g * HD : (g + 1) * HD] = o[g * rows : (g + 1) * rows].astype(o_ref.dtype)


def attend(queries, blocks, where, scale, doc_start, interpret=False):
    rows = queries.shape[0]
    width = rows * (len(blocks) - 1)
    per_group = HQ // HK
    flops = 4 * HQ * rows * width * HD
    k_specs = [pl.BlockSpec((rows, HD), lambda h: (0, h)) for _ in blocks]
    v_specs = [pl.BlockSpec((rows, HD), lambda h: (0, h + HK)) for _ in blocks]
    return pl.pallas_call(
        attend_kernel,
        grid=(HK,),
        in_specs=[
            pl.BlockSpec(memory_space=pltpu.SMEM),
            pl.BlockSpec(memory_space=pltpu.SMEM),
            pl.BlockSpec((rows, 1), lambda h: (0, 0)),
            pl.BlockSpec((rows, per_group * HD), lambda h: (0, h)),
        ]
        + k_specs
        + v_specs,
        out_specs=pl.BlockSpec((rows, per_group * HD), lambda h: (0, h)),
        out_shape=jax.ShapeDtypeStruct((rows, HQ * HD), jnp.bfloat16),
        cost_estimate=pl.CostEstimate(
            flops=flops,
            transcendentals=HQ * rows * width,
            bytes_accessed=2 * (2 * rows * HQ * HD + width * 2 * HK * HD),
        ),
        interpret=interpret,
    )(where, scale, doc_start, queries, *blocks, *blocks)


def body(queries, keys, values, lengths, ssmax_scale, far=()):
    tok_rows = queries.shape[0]
    slab_rows = tok_rows * lax.axis_size("grp")
    doc_most = WIN_DEV * tok_rows
    grp_index = lax.axis_index("grp")
    ctx_index = lax.axis_index("ctx")
    q_start = ctx_index * slab_rows + grp_index * tok_rows
    q_pos = q_start + jnp.arange(tok_rows, dtype=jnp.int32)
    own = jnp.concatenate([keys, values], axis=1)
    blocks = window_blocks(own, far)
    totals = jnp.cumsum(lengths, dtype=jnp.int32)
    before = totals[None, :] <= q_pos[:, None]
    doc_start = jnp.sum(jnp.where(before, lengths[None, :], 0), axis=1, dtype=jnp.int32)
    where = jnp.stack([q_start, grp_index % 2]).astype(jnp.int32)
    return attend(queries, blocks, where, ssmax_scale, doc_start[:, None])


def solution(mesh):
    return jax.shard_map(
        functools.partial(body, far=far_receivers(mesh)),
        mesh=mesh,
        in_specs=(
            P(AXES, None),
            P(AXES, None),
            P(AXES, None),
            P(),
            P(),
        ),
        out_specs=P(AXES, None),
        check_vma=False,
    )
```

```python
import functools

import jax
import jax.numpy as jnp
from jax import lax
from jax.experimental import pallas as pl
from jax.experimental.pallas import tpu as pltpu
from jax.sharding import PartitionSpec as P

HQ = 32
HK = 4
HD = 128
WIN_DEV = 4
AXES = ("ctx", "grp")


def send(x, pairs):
    return lax.ppermute(x, AXES, pairs)


def far_receivers(mesh):
    flat = list(mesh.devices.reshape(-1))
    try:
        chips = [tuple(d.coords) for d in flat]
    except AttributeError:
        return ()
    sizes = [max(c[a] for c in chips) + 1 for a in range(len(chips[0]))]

    def hops(a, b):
        return sum(min(abs(p - q), n - abs(p - q)) for p, q, n in zip(a, b, sizes))

    return tuple(i for i in range(4, len(flat)) if hops(chips[i - 2], chips[i]) >= 3)


def window_blocks(own, far):
    count = lax.axis_size("ctx") * lax.axis_size("grp")
    ahead2 = [(i, i + 2) for i in range(count - 2)]
    to_odd = [(i, i + 1) for i in range(0, count - 1, 2)]
    to_even = [(i, i - 1) for i in range(1, count, 2)]
    swap = to_odd + to_even
    far_set = set(far)
    back2 = send(own, ahead2)
    from_even_own = send(own, to_odd)
    direct4 = send(own, [(i - 4, i) for i in far])
    forward2 = [(i, j) for i, j in ahead2 if j not in far_set]
    back4 = send(back2, forward2) + direct4 if far else send(back2, forward2)
    swapped2 = send(back2, swap)
    from_odd4 = send(back4, to_even)
    return [back4, from_odd4, swapped2, back2, from_even_own, own]


def attend_kernel(qs_ref, scale_ref, ds_ref, q_ref, *refs):
    kv_refs, o_ref = refs[:-1], refs[-1]
    half = len(kv_refs) // 2
    rows = q_ref.shape[0]
    width = rows * (half - 1)
    doc_most = width - rows
    head = pl.program_id(0)
    q_start = qs_ref[0]
    even = qs_ref[1] == 0

    def ordered(r):
        back4, odd4, swap2, back2, even_own, own = [x[...] for x in r]
        back3 = jnp.where(even, odd4, swap2)
        back1 = jnp.where(even, swap2, even_own)
        return jnp.concatenate([back4, back3, back2, back1, own], axis=0)

    col = lax.broadcasted_iota(jnp.int32, (rows, width), 1)
    row = lax.broadcasted_iota(jnp.int32, (rows, width), 0)
    doc_start = ds_ref[...]
    live = (col >= doc_start - (q_start - doc_most)) & (col <= row + doc_most)
    bias = jnp.where(live, jnp.float32(0), -jnp.inf)
    k = ordered(kv_refs[:half])
    v = ordered(kv_refs[half:])
    q_pos = q_start + lax.broadcasted_iota(jnp.int32, (rows, 1), 0)
    logv = jnp.log((q_pos - doc_start + 1).astype(jnp.float32))
    per_group = HQ // HK
    coef = jnp.stack(
        [scale_ref[head * per_group + g] * logv / jnp.sqrt(jnp.float32(HD)) for g in range(per_group)]
    )
    q = jnp.concatenate([q_ref[:, g * HD : (g + 1) * HD] for g in range(per_group)], axis=0)
    s = lax.dot_general(q, k, (((1,), (1,)), ((), ())), preferred_element_type=jnp.float32)
    s = s.reshape(per_group, rows, width) * coef + bias[None]
    m = jnp.max(s, axis=2, keepdims=True)
    p = jnp.exp(s - m)
    l = jnp.sum(p, axis=2, keepdims=True)
    w = (p * (1.0 / l)).astype(jnp.bfloat16).reshape(per_group * rows, width)
    o = jnp.dot(w, v, preferred_element_type=jnp.float32)
    for g in range(per_group):
        o_ref[:, g * HD : (g + 1) * HD] = o[g * rows : (g + 1) * rows].astype(o_ref.dtype)


def attend(queries, blocks, where, scale, doc_start, interpret=False):
    rows = queries.shape[0]
    width = rows * (len(blocks) - 1)
    per_group = HQ // HK
    flops = 4 * HQ * rows * width * HD
    k_specs = [pl.BlockSpec((rows, HD), lambda h: (0, h)) for _ in blocks]
    v_specs = [pl.BlockSpec((rows, HD), lambda h: (0, h + HK)) for _ in blocks]
    return pl.pallas_call(
        attend_kernel,
        grid=(HK,),
        in_specs=[
            pl.BlockSpec(memory_space=pltpu.SMEM),
            pl.BlockSpec(memory_space=pltpu.SMEM),
            pl.BlockSpec((rows, 1), lambda h: (0, 0)),
            pl.BlockSpec((rows, per_group * HD), lambda h: (0, h)),
        ]
        + k_specs
        + v_specs,
        out_specs=pl.BlockSpec((rows, per_group * HD), lambda h: (0, h)),
        out_shape=jax.ShapeDtypeStruct((rows, HQ * HD), jnp.bfloat16),
        cost_estimate=pl.CostEstimate(
            flops=flops,
            transcendentals=HQ * rows * width,
            bytes_accessed=2 * (2 * rows * HQ * HD + width * 2 * HK * HD),
        ),
        interpret=interpret,
    )(where, scale, doc_start, queries, *blocks, *blocks)


def body(queries, keys, values, lengths, ssmax_scale, far=()):
    tok_rows = queries.shape[0]
    slab_rows = tok_rows * lax.axis_size("grp")
    doc_most = WIN_DEV * tok_rows
    grp_index = lax.axis_index("grp")
    ctx_index = lax.axis_index("ctx")
    q_start = ctx_index * slab_rows + grp_index * tok_rows
    q_pos = q_start + jnp.arange(tok_rows, dtype=jnp.int32)
    own = jnp.concatenate([keys, values], axis=1)
    blocks = window_blocks(own, far)
    totals = jnp.cumsum(lengths, dtype=jnp.int32)
    before = totals[None, :] <= q_pos[:, None]
    doc_start = jnp.sum(jnp.where(before, lengths[None, :], 0), axis=1, dtype=jnp.int32)
    where = jnp.stack([q_start, grp_index % 2]).astype(jnp.int32)
    return attend(queries, blocks, where, ssmax_scale, doc_start[:, None])


def solution(mesh):
    return jax.shard_map(
        functools.partial(body, far=far_receivers(mesh)),
        mesh=mesh,
        in_specs=(
            P(AXES, None),
            P(AXES, None),
            P(AXES, None),
            P(),
            P(),
        ),
        out_specs=P(AXES, None),
        check_vma=False,
    )
```

```python
import functools

import jax
import jax.numpy as jnp
from jax import lax
from jax.experimental import pallas as pl
from jax.experimental.pallas import tpu as pltpu
from jax.sharding import PartitionSpec as P

HQ = 32
HK = 4
HD = 128
WIN_DEV = 4
SPLIT = 2
AXES = ("ctx", "grp")


def send(x, pairs):
    return lax.ppermute(x, AXES, pairs)


def far_receivers(mesh):
    flat = list(mesh.devices.reshape(-1))
    try:
        chips = [tuple(d.coords) for d in flat]
    except AttributeError:
        return ()
    sizes = [max(c[a] for c in chips) + 1 for a in range(len(chips[0]))]

    def hops(a, b):
        return sum(min(abs(p - q), n - abs(p - q)) for p, q, n in zip(a, b, sizes))

    return tuple(i for i in range(4, len(flat)) if hops(chips[i - 2], chips[i]) >= 3)


def window_blocks(own, far):
    count = lax.axis_size("ctx") * lax.axis_size("grp")
    ahead2 = [(i, i + 2) for i in range(count - 2)]
    to_odd = [(i, i + 1) for i in range(0, count - 1, 2)]
    to_even = [(i, i - 1) for i in range(1, count, 2)]
    swap = to_odd + to_even
    far_set = set(far)
    back2 = send(own, ahead2)
    from_even_own = send(own, to_odd)
    direct4 = send(own, [(i - 4, i) for i in far])
    forward2 = [(i, j) for i, j in ahead2 if j not in far_set]
    back4 = send(back2, forward2) + direct4 if far else send(back2, forward2)
    swapped2 = send(back2, swap)
    from_odd4 = send(back4, to_even)
    return [back4, from_odd4, swapped2, back2, from_even_own, own]


def attend_kernel(qs_ref, scale_ref, ds_ref, q_ref, *refs):
    kv_refs, o_ref = refs[:-1], refs[-1]
    half = len(kv_refs) // 2
    rows = q_ref.shape[0]
    width = rows * (half - 1)
    doc_most = width - rows
    head = pl.program_id(0)
    part = pl.program_id(1)
    q_start = qs_ref[0]
    even = qs_ref[1] == 0

    def ordered(r):
        back4, odd4, swap2, back2, even_own, own = [x[...] for x in r]
        back3 = jnp.where(even, odd4, swap2)
        back1 = jnp.where(even, swap2, even_own)
        return jnp.concatenate([back4, back3, back2, back1, own], axis=0)

    col = lax.broadcasted_iota(jnp.int32, (rows, width), 1)
    row = lax.broadcasted_iota(jnp.int32, (rows, width), 0)
    doc_start = ds_ref[...]
    live = (col >= doc_start - (q_start - doc_most)) & (col <= row + doc_most)
    k = ordered(kv_refs[:half])
    v = ordered(kv_refs[half:])
    q_pos = q_start + lax.broadcasted_iota(jnp.int32, (rows, 1), 0)
    logv = jnp.log((q_pos - doc_start + 1).astype(jnp.float32))
    per_group = HQ // HK // SPLIT
    coef = jnp.stack(
        [scale_ref[(head * SPLIT + part) * per_group + g] * logv / jnp.sqrt(jnp.float32(HD)) for g in range(per_group)]
    )
    q = jnp.concatenate([q_ref[:, g * HD : (g + 1) * HD] for g in range(per_group)], axis=0)
    s = lax.dot_general(q, k, (((1,), (1,)), ((), ())), preferred_element_type=jnp.float32)
    s = jnp.where(live[None], s.reshape(per_group, rows, width) * coef, -jnp.inf)
    m = jnp.max(s, axis=2, keepdims=True)
    p = jnp.exp(s - m)
    l = jnp.sum(p, axis=2, keepdims=True)
    w = (p * (1.0 / l)).astype(jnp.bfloat16).reshape(per_group * rows, width)
    o = jnp.dot(w, v, preferred_element_type=jnp.float32)
    for g in range(per_group):
        o_ref[:, g * HD : (g + 1) * HD] = o[g * rows : (g + 1) * rows].astype(o_ref.dtype)


def attend(queries, blocks, where, scale, doc_start, interpret=False):
    rows = queries.shape[0]
    width = rows * (len(blocks) - 1)
    per_group = HQ // HK // SPLIT
    flops = 4 * HQ * rows * width * HD
    k_specs = [pl.BlockSpec((rows, HD), lambda h, j: (0, h)) for _ in blocks]
    v_specs = [pl.BlockSpec((rows, HD), lambda h, j: (0, h + HK)) for _ in blocks]
    return pl.pallas_call(
        attend_kernel,
        grid=(HK, SPLIT),
        in_specs=[
            pl.BlockSpec(memory_space=pltpu.SMEM),
            pl.BlockSpec(memory_space=pltpu.SMEM),
            pl.BlockSpec((rows, 1), lambda h, j: (0, 0)),
            pl.BlockSpec((rows, per_group * HD), lambda h, j: (0, h * SPLIT + j)),
        ]
        + k_specs
        + v_specs,
        out_specs=pl.BlockSpec((rows, per_group * HD), lambda h, j: (0, h * SPLIT + j)),
        out_shape=jax.ShapeDtypeStruct((rows, HQ * HD), jnp.bfloat16),
        cost_estimate=pl.CostEstimate(
            flops=flops,
            transcendentals=HQ * rows * width,
            bytes_accessed=2 * (2 * rows * HQ * HD + width * 2 * HK * HD),
        ),
        interpret=interpret,
    )(where, scale, doc_start, queries, *blocks, *blocks)


def body(queries, keys, values, lengths, ssmax_scale, far=()):
    tok_rows = queries.shape[0]
    slab_rows = tok_rows * lax.axis_size("grp")
    doc_most = WIN_DEV * tok_rows
    grp_index = lax.axis_index("grp")
    ctx_index = lax.axis_index("ctx")
    q_start = ctx_index * slab_rows + grp_index * tok_rows
    q_pos = q_start + jnp.arange(tok_rows, dtype=jnp.int32)
    own = jnp.concatenate([keys, values], axis=1)
    blocks = window_blocks(own, far)
    totals = jnp.cumsum(lengths, dtype=jnp.int32)
    before = totals[None, :] <= q_pos[:, None]
    doc_start = jnp.sum(jnp.where(before, lengths[None, :], 0), axis=1, dtype=jnp.int32)
    where = jnp.stack([q_start, grp_index % 2]).astype(jnp.int32)
    return attend(queries, blocks, where, ssmax_scale, doc_start[:, None])


def solution(mesh):
    return jax.shard_map(
        functools.partial(body, far=far_receivers(mesh)),
        mesh=mesh,
        in_specs=(
            P(AXES, None),
            P(AXES, None),
            P(AXES, None),
            P(),
            P(),
        ),
        out_specs=P(AXES, None),
        check_vma=False,
    )
```
